128 devices in a mesh: gx: 32 (over x, y_lo, z), gy: 4 (over y_hi, core).
Axes of the slice: x: 4, y: 4 (y_hi: 2, y_lo: 2; y = y_hi * 2 + y_lo), z: 4, core: 2. Of those that a mesh axis runs over, the one named last changes fastest.
Arguments:
- field_in: bfloat16 [20, 128, 128, 1024], P(None, 'gx', 'gy'), may hold values from -6 to 6
- cotangent: bfloat16 [20, 128, 128, 1024], P(None, 'gx', 'gy'), may hold values from -6 to 6
- spec_weight: float32 [2, 192, 20, 20, 24, 24], P(None, 'gx', None, None, 'gy'), may hold values from -6 to 6
Outputs:
- grad_field: bfloat16 [20, 128, 128, 1024], P(None, 'gx', 'gy')
- grad_weight: float32 [2, 192, 20, 20, 24, 24], P(None, 'gx', None, None, 'gy')
The draws below stay inside these ranges and needn't reach their ends.
All inputs are finite; a program needn't handle non-finite values.
Results may differ from the reference program's by a relative error of at most 0.001.
Values sent between devices are 32-bit elements; how exact they have to be, the bound alone decides.
No kernel may reach another device: no remote copies, remote signals or barrier semaphores. Data moves between devices by JAX's collectives and lax.ppermute only.
A program may use at most 512 MiB of HBM per device.

```python
import math
import jax
import jax.numpy as jnp
from jax import lax

C = 20
MX = 12
MY = 12
MZ = 12
MT = 8
Z = 64
T_SIZE = 16
X = 128
Y = 128
ZT = 1024
KX = 24
KY = 24
M = 192


def shard_levels(own_key, shape, split, smallest, top_value):
    def one(axis_at, parts):
        steps = jax.random.uniform(jax.random.fold_in(jax.random.fold_in(own_key, 6), axis_at), (parts,), jnp.float32, smallest / len(split), top_value / len(split))
        return jnp.repeat(jnp.exp(steps), shape[axis_at] // parts).reshape((-1,) + (1,) * (len(shape) - axis_at - 1))

    loudness = one(*split[0])
    for cut in split[1:]:
        loudness = loudness * one(*cut)
    return loudness


def centred(key, extent, spread, bound, shards=(), kind=jnp.bfloat16):
    loudness = shard_levels(key, extent, shards, -0.22, 0.18) if shards else 1.0
    result = jax.random.normal(key, extent, jnp.float32) * spread * loudness
    return jnp.minimum(jnp.maximum(result, -bound), bound).astype(kind)


def setup_inputs(seed: int = 0) -> dict:
    streams_of = jax.random.split(jax.random.key(seed), 4)
    return {
        "field_in": centred(streams_of[0], (C, X, Y, ZT), 1.0, 6.0, ((1, 32), (2, 4))),
        "cotangent": centred(streams_of[1], (C, X, Y, ZT), 1.0, 6.0, ((1, 32), (2, 4))),
        "spec_weight": centred(streams_of[2], (2, M, C, C, KX, KY), 1.0, 6.0, ((1, 32), (4, 4)), jnp.float32),
    }


def keep_modes(values, half_count, along_axis, length):
    lower_part = lax.slice_in_dim(values, 0, half_count, axis=along_axis)
    upper_part = lax.slice_in_dim(values, length - half_count, length, axis=along_axis)
    return jnp.concatenate([lower_part, upper_part], along_axis)

def place_modes(values, half_count, along_axis, length):
    lower_part = lax.slice_in_dim(values, 0, half_count, axis=along_axis)
    upper_part = lax.slice_in_dim(values, half_count, 2 * half_count, axis=along_axis)
    pad_shape = list(values.shape)
    pad_shape[along_axis] = length - 2 * half_count
    return jnp.concatenate([lower_part, jnp.zeros(pad_shape, values.dtype), upper_part], along_axis)

def spectrum(field):
    norm_factor = 1.0 / math.sqrt(X * Y * Z * T_SIZE)

    def channel_spectrum(plane):
        volume = plane.astype(jnp.float32).reshape(X, Y, Z, T_SIZE)
        coeffs = jnp.fft.rfftn(volume)
        coeffs = keep_modes(coeffs, MX, 0, X)
        coeffs = keep_modes(coeffs, MY, 1, Y)
        coeffs = keep_modes(coeffs, MZ, 2, Z)
        coeffs = coeffs[:, :, :, :MT].reshape(KX, KY, M) * norm_factor
        return jnp.stack([jnp.real(coeffs), jnp.imag(coeffs)])
    return jnp.transpose(lax.map(channel_spectrum, field), (1, 4, 0, 2, 3))

def reference(field_in, cotangent, spec_weight):
    forward_field = spectrum(field_in)
    forward_dual = spectrum(cotangent)
    doubling = jnp.where(jnp.arange(M) % MT == 0, 1.0, 2.0).astype(jnp.float32)
    widened = doubling[:, None, None, None]
    dual_real = forward_dual[0] * widened
    dual_imag = forward_dual[1] * widened
    field_real = forward_field[0]
    field_imag = forward_field[1]
    grad_real = field_real[:, :, None] * dual_real[:, None] + field_imag[:, :, None] * dual_imag[:, None]
    grad_imag = field_real[:, :, None] * dual_imag[:, None] - field_imag[:, :, None] * dual_real[:, None]
    grad_weight = jnp.stack([grad_real, grad_imag])
    back_real = lax.optimization_barrier(jnp.sum(spec_weight[0] * dual_real[:, None] + spec_weight[1] * dual_imag[:, None], axis=2))
    back_imag = lax.optimization_barrier(jnp.sum(spec_weight[0] * dual_imag[:, None] - spec_weight[1] * dual_real[:, None], axis=2))
    backward = jnp.transpose(jnp.stack([back_real, back_imag]), (2, 0, 3, 4, 1))
    norm_factor = math.sqrt(X * Y * Z * T_SIZE)

    def channel_field(paired):
        values = lax.complex(paired[0] / doubling, paired[1] / doubling).reshape(KX, KY, 2 * MZ, MT)
        values = place_modes(values, MX, 0, X)
        values = place_modes(values, MY, 1, Y)
        values = place_modes(values, MZ, 2, Z)
        pad_shape = (X, Y, Z, T_SIZE // 2 + 1 - MT)
        values = jnp.concatenate([values, jnp.zeros(pad_shape, values.dtype)], 3)
        volume = jnp.fft.irfftn(values, s=(X, Y, Z, T_SIZE)) * norm_factor
        return volume.reshape(X, Y, Z * T_SIZE)
    grad_field = lax.map(channel_field, backward)
    return (grad_field.astype(jnp.bfloat16), grad_weight)
```

```python
import math

import jax
import jax.numpy as jnp
from jax import lax
from jax.sharding import PartitionSpec as P

MX = 12
MY = 12
MZ = 12
MT = 8
Z = 64
T_SIZE = 16
KX = 24
KY = 24
M = 192


exact_precision = lax.Precision.HIGHEST
split_precision = lax.Precision.HIGH
lead_contract = (((0,), (0,)), ((), ()))
tail_contract = (((1,), (1,)), ((), ()))


def signed_freqs(count, half_count):
    ladder = lax.iota(jnp.int32, count)
    return jnp.where(ladder < half_count, ladder, ladder - 2 * half_count)


def pair_table(frequencies, length):
    places = lax.iota(jnp.int32, length)
    residue = jnp.remainder(frequencies[:, None] * places[None, :], length)
    phases = residue.astype(jnp.float32) * (2.0 * math.pi / length)
    cosine = jnp.cos(phases) / math.sqrt(length)
    sines = jnp.sin(phases) / math.sqrt(length)
    return jnp.stack([jnp.stack([cosine, sines]), jnp.stack([-sines, cosine])])


def depth_rows_table():
    cell_ids = lax.iota(jnp.int32, Z * T_SIZE)
    depth_index = cell_ids // T_SIZE
    time_index = cell_ids % T_SIZE
    mode_ids = lax.iota(jnp.int32, M)
    depth_freq = mode_ids // MT
    depth_freq = jnp.where(depth_freq < MZ, depth_freq, depth_freq - 2 * MZ)
    time_freq = mode_ids % MT
    residue = jnp.remainder(
        depth_freq[:, None] * depth_index[None, :] * T_SIZE
        + time_freq[:, None] * time_index[None, :] * Z,
        Z * T_SIZE,
    )
    phases = residue.astype(jnp.float32) * (2.0 * math.pi / (Z * T_SIZE))
    factor = 1.0 / math.sqrt(Z * T_SIZE)
    return jnp.stack([jnp.cos(phases) * factor, -jnp.sin(phases) * factor])


def split_table(table):
    leading = table.astype(jnp.bfloat16)
    residual_part = (table - lax.optimization_barrier(leading).astype(jnp.float32)).astype(
        jnp.bfloat16
    )
    return (leading, residual_part)


def per_device(field_in, cotangent, spec_weight):
    channels, x_local, y_local, depth_time = field_in.shape
    x_groups = lax.axis_size("gx")
    x_count = x_local * x_groups
    y_count = y_local * lax.axis_size("gy")
    mode_local = M // x_groups
    x_table = pair_table(signed_freqs(KX, MX), x_count)
    x_blocks = x_table.reshape(2, 2, KX, x_groups, x_local)
    y_table = pair_table(signed_freqs(KY, MY), y_count)
    depth_modes = depth_rows_table()
    depth_flat = depth_modes.reshape(2 * M, depth_time)
    depth_lead, depth_tail = split_table(depth_flat)

    def depth_forward(flat_rows):
        first = lax.dot_general(
            depth_lead, flat_rows, tail_contract, preferred_element_type=jnp.float32
        )
        return first + lax.dot_general(
            depth_tail, flat_rows, tail_contract, preferred_element_type=jnp.float32
        )

    def field_modes(field):
        spectra = depth_forward(field.reshape(-1, depth_time)).reshape(
            2, x_groups, mode_local, channels, x_local * y_local
        )
        section = lax.all_to_all(spectra, "gx", split_axis=1, concat_axis=1, tiled=True)
        planes = section.reshape(section.shape[:4] + (x_local, y_local))
        regrouped = jnp.einsum("pqkbx,qbjcxy->pjcky", x_blocks, planes, precision=split_precision)
        return jnp.einsum(
            "pqky,qjcay->pjcak",
            y_table,
            lax.all_to_all(regrouped, "gy", split_axis=3, concat_axis=4, tiled=True),
            precision=split_precision,
        )

    at_modes = jnp.stack([field_modes(field_in), field_modes(cotangent)])
    mode_ids = lax.axis_index("gx") * mode_local + lax.iota(jnp.int32, mode_local)
    doubling = jnp.where(mode_ids % MT == 0, 1.0, 2.0).astype(jnp.float32)[:, None, None, None]
    field_real = at_modes[0, 0]
    field_imag = at_modes[0, 1]
    dual_real = at_modes[1, 0] * doubling
    dual_imag = at_modes[1, 1] * doubling
    grad_real = (
        field_real[:, :, None] * dual_real[:, None] + field_imag[:, :, None] * dual_imag[:, None]
    )
    grad_imag = (
        field_real[:, :, None] * dual_imag[:, None] - field_imag[:, :, None] * dual_real[:, None]
    )
    grad_weight = jnp.stack([grad_real, grad_imag])
    back_real = jnp.sum(
        spec_weight[0] * dual_real[:, None] + spec_weight[1] * dual_imag[:, None], axis=2
    )
    back_imag = jnp.sum(
        spec_weight[0] * dual_imag[:, None] - spec_weight[1] * dual_real[:, None], axis=2
    )
    backward = jnp.stack([back_real, back_imag])
    spread = jnp.einsum("qpky,qjcak->pjcay", y_table, backward, precision=split_precision)
    y_done = lax.all_to_all(spread, "gy", split_axis=4, concat_axis=3, tiled=True)
    x_spread = jnp.einsum("qpkbx,qjcky->pjcbxy", x_blocks, y_done, precision=split_precision)
    section = lax.all_to_all(x_spread, "gx", split_axis=3, concat_axis=1, tiled=True)
    rows = section.reshape(section.shape[0] * section.shape[1], -1)
    summed = lax.dot_general(rows, depth_flat, lead_contract, precision=split_precision)
    grad_field = summed.reshape(section.shape[2], x_local, y_local, depth_time)
    return (grad_field.astype(jnp.bfloat16), grad_weight)


def solution(mesh):
    in_specs = (
        P(None, "gx", "gy", None),
        P(None, "gx", "gy", None),
        P(None, "gx", None, None, "gy", None),
    )
    out_specs = (P(None, "gx", "gy", None), P(None, "gx", None, None, "gy", None))
    return jax.shard_map(
        per_device, mesh=mesh, in_specs=in_specs, out_specs=out_specs, check_vma=False
    )
```

```python
import math

import jax
import jax.numpy as jnp
from jax import lax
from jax.sharding import PartitionSpec as P

MX = 12
MY = 12
MZ = 12
MT = 8
Z = 64
T_SIZE = 16
KX = 24
KY = 24
M = 192


exact_precision = lax.Precision.HIGHEST
split_precision = lax.Precision.HIGH
lead_contract = (((0,), (0,)), ((), ()))
tail_contract = (((1,), (1,)), ((), ()))


def signed_freqs(count, half_count):
    ladder = lax.iota(jnp.int32, count)
    return jnp.where(ladder < half_count, ladder, ladder - 2 * half_count)


def pair_table(frequencies, length):
    places = lax.iota(jnp.int32, length)
    residue = jnp.remainder(frequencies[:, None] * places[None, :], length)
    phases = residue.astype(jnp.float32) * (2.0 * math.pi / length)
    cosine = jnp.cos(phases) / math.sqrt(length)
    sines = jnp.sin(phases) / math.sqrt(length)
    return jnp.stack([jnp.stack([cosine, sines]), jnp.stack([-sines, cosine])])


def depth_rows_table():
    cell_ids = lax.iota(jnp.int32, Z * T_SIZE)
    depth_index = cell_ids // T_SIZE
    time_index = cell_ids % T_SIZE
    mode_ids = lax.iota(jnp.int32, M)
    depth_freq = mode_ids // MT
    depth_freq = jnp.where(depth_freq < MZ, depth_freq, depth_freq - 2 * MZ)
    time_freq = mode_ids % MT
    residue = jnp.remainder(
        depth_freq[:, None] * depth_index[None, :] * T_SIZE
        + time_freq[:, None] * time_index[None, :] * Z,
        Z * T_SIZE,
    )
    phases = residue.astype(jnp.float32) * (2.0 * math.pi / (Z * T_SIZE))
    factor = 1.0 / math.sqrt(Z * T_SIZE)
    return jnp.stack([jnp.cos(phases) * factor, -jnp.sin(phases) * factor])


def split_table(table):
    leading = table.astype(jnp.bfloat16)
    residual_part = (table - lax.optimization_barrier(leading).astype(jnp.float32)).astype(
        jnp.bfloat16
    )
    return (leading, residual_part)


def local_pair_table(frequencies, length, offset, count):
    places = offset + lax.iota(jnp.int32, count)
    residue = jnp.remainder(frequencies[:, None] * places[None, :], length)
    phases = residue.astype(jnp.float32) * (2.0 * math.pi / length)
    cosine = jnp.cos(phases) / math.sqrt(length)
    sines = jnp.sin(phases) / math.sqrt(length)
    return jnp.stack([jnp.stack([cosine, sines]), jnp.stack([-sines, cosine])])


def per_device(field_in, cotangent, spec_weight):
    channels, x_local, y_local, depth_time = field_in.shape
    x_groups = lax.axis_size("gx")
    x_count = x_local * x_groups
    y_count = y_local * lax.axis_size("gy")
    mode_local = M // x_groups
    x_table = pair_table(signed_freqs(KX, MX), x_count)
    x_blocks = x_table.reshape(2, 2, KX, x_groups, x_local)
    y_start = lax.axis_index("gy") * y_local
    y_near = local_pair_table(signed_freqs(KY, MY), y_count, y_start, y_local)
    depth_modes = depth_rows_table()
    depth_flat = depth_modes.reshape(2 * M, depth_time)
    depth_lead, depth_tail = split_table(depth_flat)

    def depth_forward(flat_rows):
        first = lax.dot_general(
            depth_lead, flat_rows, tail_contract, preferred_element_type=jnp.float32
        )
        return first + lax.dot_general(
            depth_tail, flat_rows, tail_contract, preferred_element_type=jnp.float32
        )

    def field_modes(field):
        spectra = depth_forward(field.reshape(-1, depth_time)).reshape(
            2, M, channels, x_local, y_local
        )
        partial_y = jnp.einsum("pqky,qmcxy->mpcxk", y_near, spectra, precision=split_precision)
        partial_y = partial_y.reshape((x_groups, mode_local) + partial_y.shape[1:])
        section = lax.all_to_all(partial_y, "gx", split_axis=0, concat_axis=0, tiled=True)
        summed_x = jnp.einsum("pqkbx,bjqcxl->pjckl", x_blocks, section, precision=split_precision)
        return lax.psum_scatter(summed_x, "gy", scatter_dimension=3, tiled=True)

    at_modes = jnp.stack([field_modes(field_in), field_modes(cotangent)])
    mode_ids = lax.axis_index("gx") * mode_local + lax.iota(jnp.int32, mode_local)
    doubling = jnp.where(mode_ids % MT == 0, 1.0, 2.0).astype(jnp.float32)[:, None, None, None]
    field_real = at_modes[0, 0]
    field_imag = at_modes[0, 1]
    dual_real = at_modes[1, 0] * doubling
    dual_imag = at_modes[1, 1] * doubling
    grad_real = (
        field_real[:, :, None] * dual_real[:, None] + field_imag[:, :, None] * dual_imag[:, None]
    )
    grad_imag = (
        field_real[:, :, None] * dual_imag[:, None] - field_imag[:, :, None] * dual_real[:, None]
    )
    grad_weight = jnp.stack([grad_real, grad_imag])
    back_real = jnp.sum(
        spec_weight[0] * dual_real[:, None] + spec_weight[1] * dual_imag[:, None], axis=2
    )
    back_imag = jnp.sum(
        spec_weight[0] * dual_imag[:, None] - spec_weight[1] * dual_real[:, None], axis=2
    )
    backward = jnp.stack([back_real, back_imag])
    all_x = lax.all_gather(backward, "gy", axis=3, tiled=True)
    x_spread = jnp.einsum("qpkbx,qjckl->bpjcxl", x_blocks, all_x, precision=split_precision)
    section = lax.all_to_all(x_spread, "gx", split_axis=0, concat_axis=0, tiled=True)
    rows = jnp.einsum("qpky,sqjcxk->psjcxy", y_near, section, precision=split_precision)
    rows = rows.reshape(2 * M, -1)
    summed = lax.dot_general(rows, depth_flat, lead_contract, precision=split_precision)
    grad_field = summed.reshape(channels, x_local, y_local, depth_time)
    return (grad_field.astype(jnp.bfloat16), grad_weight)


def solution(mesh):
    in_specs = (
        P(None, "gx", "gy", None),
        P(None, "gx", "gy", None),
        P(None, "gx", None, None, "gy", None),
    )
    out_specs = (P(None, "gx", "gy", None), P(None, "gx", None, None, "gy", None))
    return jax.shard_map(
        per_device, mesh=mesh, in_specs=in_specs, out_specs=out_specs, check_vma=False
    )
```

```python
import math

import jax
import jax.numpy as jnp
from jax import lax
from jax.sharding import PartitionSpec as P

MX = 12
MY = 12
MZ = 12
MT = 8
Z = 64
T_SIZE = 16
KX = 24
KY = 24
M = 192


exact_precision = lax.Precision.HIGHEST
split_precision = lax.Precision.HIGH
lead_contract = (((0,), (0,)), ((), ()))
tail_contract = (((1,), (1,)), ((), ()))


def signed_freqs(count, half_count):
    ladder = lax.iota(jnp.int32, count)
    return jnp.where(ladder < half_count, ladder, ladder - 2 * half_count)


def pair_table(frequencies, length):
    places = lax.iota(jnp.int32, length)
    residue = jnp.remainder(frequencies[:, None] * places[None, :], length)
    phases = residue.astype(jnp.float32) * (2.0 * math.pi / length)
    cosine = jnp.cos(phases) / math.sqrt(length)
    sines = jnp.sin(phases) / math.sqrt(length)
    return jnp.stack([jnp.stack([cosine, sines]), jnp.stack([-sines, cosine])])


def depth_rows_table():
    cell_ids = lax.iota(jnp.int32, Z * T_SIZE)
    depth_index = cell_ids // T_SIZE
    time_index = cell_ids % T_SIZE
    mode_ids = lax.iota(jnp.int32, M)
    depth_freq = mode_ids // MT
    depth_freq = jnp.where(depth_freq < MZ, depth_freq, depth_freq - 2 * MZ)
    time_freq = mode_ids % MT
    residue = jnp.remainder(
        depth_freq[:, None] * depth_index[None, :] * T_SIZE
        + time_freq[:, None] * time_index[None, :] * Z,
        Z * T_SIZE,
    )
    phases = residue.astype(jnp.float32) * (2.0 * math.pi / (Z * T_SIZE))
    factor = 1.0 / math.sqrt(Z * T_SIZE)
    return jnp.stack([jnp.cos(phases) * factor, -jnp.sin(phases) * factor])


def split_table(table):
    leading = table.astype(jnp.bfloat16)
    residual_part = (table - lax.optimization_barrier(leading).astype(jnp.float32)).astype(
        jnp.bfloat16
    )
    return (leading, residual_part)


def per_device(field_in, cotangent, spec_weight):
    channels, x_local, y_local, depth_time = field_in.shape
    x_groups = lax.axis_size("gx")
    x_count = x_local * x_groups
    y_count = y_local * lax.axis_size("gy")
    mode_local = M // x_groups
    x_table = pair_table(signed_freqs(KX, MX), x_count)
    x_blocks = x_table.reshape(2, 2, KX, x_groups, x_local)
    y_table = pair_table(signed_freqs(KY, MY), y_count)
    depth_modes = depth_rows_table()
    depth_flat = depth_modes.reshape(2 * M, depth_time)
    depth_lead, depth_tail = split_table(depth_flat)

    def depth_forward(flat_rows):
        first = lax.dot_general(
            depth_lead, flat_rows, tail_contract, preferred_element_type=jnp.float32
        )
        return first + lax.dot_general(
            depth_tail, flat_rows, tail_contract, preferred_element_type=jnp.float32
        )

    def field_modes(field):
        spectra = depth_forward(field.reshape(-1, depth_time)).reshape(
            2, x_groups, mode_local, channels, x_local * y_local
        )
        section = lax.all_to_all(spectra, "gx", split_axis=1, concat_axis=1, tiled=True)
        planes = section.reshape(section.shape[:4] + (x_local, y_local))
        regrouped = jnp.einsum("pqkbx,qbjcxy->pjcky", x_blocks, planes, precision=split_precision)
        return jnp.einsum(
            "pqky,qjcay->pjcak",
            y_table,
            lax.all_to_all(regrouped, "gy", split_axis=3, concat_axis=4, tiled=True),
            precision=split_precision,
        )

    at_modes = jnp.stack([field_modes(field_in), field_modes(cotangent)])
    mode_ids = lax.axis_index("gx") * mode_local + lax.iota(jnp.int32, mode_local)
    doubling = jnp.where(mode_ids % MT == 0, 1.0, 2.0).astype(jnp.float32)[:, None, None, None]
    field_real = at_modes[0, 0]
    field_imag = at_modes[0, 1]
    dual_real = at_modes[1, 0] * doubling
    dual_imag = at_modes[1, 1] * doubling
    grad_real = (
        field_real[:, :, None] * dual_real[:, None] + field_imag[:, :, None] * dual_imag[:, None]
    )
    grad_imag = (
        field_real[:, :, None] * dual_imag[:, None] - field_imag[:, :, None] * dual_real[:, None]
    )
    grad_weight = jnp.stack([grad_real, grad_imag])
    back_real = jnp.sum(
        spec_weight[0] * dual_real[:, None] + spec_weight[1] * dual_imag[:, None], axis=2
    )
    back_imag = jnp.sum(
        spec_weight[0] * dual_imag[:, None] - spec_weight[1] * dual_real[:, None], axis=2
    )
    backward = jnp.stack([back_real, back_imag])
    y_parts = lax.axis_size("gy")
    y_chunks = y_table.reshape(2, 2, KY, y_parts, y_local)
    spread = jnp.einsum("qpkdy,qjcak->dpajcy", y_chunks, backward, precision=split_precision)
    spread = spread.reshape(spread.shape[:4] + (channels * y_local,))
    y_done = lax.all_to_all(spread, "gy", split_axis=0, concat_axis=0, tiled=True)
    x_inverse = x_table.reshape(2, 2, y_parts, KX // y_parts, x_groups, x_local)
    x_spread = jnp.einsum("pqsabx,spajn->bxqjn", x_inverse, y_done, precision=split_precision)
    section = lax.all_to_all(x_spread, "gx", split_axis=0, concat_axis=0, tiled=True)
    depth_parts = depth_flat.reshape(2, x_groups, mode_local, depth_time)
    summed = jnp.einsum("sxqjn,qsjz->xnz", section, depth_parts, precision=split_precision)
    grad_field = summed.reshape(x_local, channels, y_local, depth_time).transpose(1, 0, 2, 3)
    return (grad_field.astype(jnp.bfloat16), grad_weight)


def solution(mesh):
    in_specs = (
        P(None, "gx", "gy", None),
        P(None, "gx", "gy", None),
        P(None, "gx", None, None, "gy", None),
    )
    out_specs = (P(None, "gx", "gy", None), P(None, "gx", None, None, "gy", None))
    return jax.shard_map(
        per_device, mesh=mesh, in_specs=in_specs, out_specs=out_specs, check_vma=False
    )
```

```python
import math

import jax
import jax.numpy as jnp
from jax import lax
from jax.sharding import PartitionSpec as P

MX = 12
MY = 12
MZ = 12
MT = 8
Z = 64
T_SIZE = 16
KX = 24
KY = 24
M = 192


exact_precision = lax.Precision.HIGHEST
split_precision = lax.Precision.HIGH
lead_contract = (((0,), (0,)), ((), ()))
tail_contract = (((1,), (1,)), ((), ()))


def signed_freqs(count, half_count):
    ladder = lax.iota(jnp.int32, count)
    return jnp.where(ladder < half_count, ladder, ladder - 2 * half_count)


def pair_table(frequencies, length):
    places = lax.iota(jnp.int32, length)
    residue = jnp.remainder(frequencies[:, None] * places[None, :], length)
    phases = residue.astype(jnp.float32) * (2.0 * math.pi / length)
    cosine = jnp.cos(phases) / math.sqrt(length)
    sines = jnp.sin(phases) / math.sqrt(length)
    return jnp.stack([jnp.stack([cosine, sines]), jnp.stack([-sines, cosine])])


def depth_rows_table():
    cell_ids = lax.iota(jnp.int32, Z * T_SIZE)
    depth_index = cell_ids // T_SIZE
    time_index = cell_ids % T_SIZE
    mode_ids = lax.iota(jnp.int32, M)
    depth_freq = mode_ids // MT
    depth_freq = jnp.where(depth_freq < MZ, depth_freq, depth_freq - 2 * MZ)
    time_freq = mode_ids % MT
    residue = jnp.remainder(
        depth_freq[:, None] * depth_index[None, :] * T_SIZE
        + time_freq[:, None] * time_index[None, :] * Z,
        Z * T_SIZE,
    )
    phases = residue.astype(jnp.float32) * (2.0 * math.pi / (Z * T_SIZE))
    factor = 1.0 / math.sqrt(Z * T_SIZE)
    return jnp.stack([jnp.cos(phases) * factor, -jnp.sin(phases) * factor])


def split_table(table):
    leading = table.astype(jnp.bfloat16)
    residual_part = (table - lax.optimization_barrier(leading).astype(jnp.float32)).astype(
        jnp.bfloat16
    )
    return (leading, residual_part)


def per_device(field_in, cotangent, spec_weight):
    channels, x_local, y_local, depth_time = field_in.shape
    x_groups = lax.axis_size("gx")
    x_count = x_local * x_groups
    y_count = y_local * lax.axis_size("gy")
    mode_local = M // x_groups
    x_table = pair_table(signed_freqs(KX, MX), x_count)
    x_blocks = x_table.reshape(2, 2, KX, x_groups, x_local)
    y_table = pair_table(signed_freqs(KY, MY), y_count)
    depth_modes = depth_rows_table()
    depth_flat = depth_modes.reshape(2 * M, depth_time)
    depth_lead, depth_tail = split_table(depth_flat)

    def depth_forward(flat_rows):
        first = lax.dot_general(
            depth_lead, flat_rows, tail_contract, preferred_element_type=jnp.float32
        )
        return first + lax.dot_general(
            depth_tail, flat_rows, tail_contract, preferred_element_type=jnp.float32
        )

    def field_modes(field):
        spectra = depth_forward(field.reshape(-1, depth_time)).reshape(
            2, x_groups, mode_local, channels, x_local * y_local
        )
        section = lax.all_to_all(spectra, "gx", split_axis=1, concat_axis=1, tiled=True)
        planes = section.reshape(section.shape[:4] + (x_local, y_local))
        regrouped = jnp.einsum("pqkbx,qbjcxy->pjcky", x_blocks, planes, precision=split_precision)
        return jnp.einsum(
            "pqky,qjcay->pjcak",
            y_table,
            lax.all_to_all(regrouped, "gy", split_axis=3, concat_axis=4, tiled=True),
            precision=split_precision,
        )

    at_modes = jnp.stack([field_modes(field_in), field_modes(cotangent)])
    mode_ids = lax.axis_index("gx") * mode_local + lax.iota(jnp.int32, mode_local)
    doubling = jnp.where(mode_ids % MT == 0, 1.0, 2.0).astype(jnp.float32)[:, None, None, None]
    field_real = at_modes[0, 0]
    field_imag = at_modes[0, 1]
    dual_real = at_modes[1, 0] * doubling
    dual_imag = at_modes[1, 1] * doubling
    grad_real = (
        field_real[:, :, None] * dual_real[:, None] + field_imag[:, :, None] * dual_imag[:, None]
    )
    grad_imag = (
        field_real[:, :, None] * dual_imag[:, None] - field_imag[:, :, None] * dual_real[:, None]
    )
    grad_weight = jnp.stack([grad_real, grad_imag])
    back_real = jnp.sum(
        spec_weight[0] * dual_real[:, None] + spec_weight[1] * dual_imag[:, None], axis=2
    )
    back_imag = jnp.sum(
        spec_weight[0] * dual_imag[:, None] - spec_weight[1] * dual_real[:, None], axis=2
    )
    backward = jnp.stack([back_real, back_imag])
    y_parts = lax.axis_size("gy")
    y_chunks = y_table.reshape(2, 2, KY, y_parts, y_local)
    spread = jnp.einsum("qpkdy,qjcak->dpajcy", y_chunks, backward, precision=split_precision)
    spread = spread.reshape(spread.shape[:4] + (channels * y_local,))
    y_done = lax.all_to_all(spread, "gy", split_axis=0, concat_axis=0, tiled=True)
    x_inverse = x_table.reshape(2, 2, y_parts, KX // y_parts, x_groups, x_local)
    x_spread = jnp.einsum("pqsabx,spajn->bxqjn", x_inverse, y_done, precision=split_precision)
    section = lax.all_to_all(x_spread, "gx", split_axis=0, concat_axis=0, tiled=True)
    depth_parts = depth_flat.reshape(2, x_groups, mode_local, depth_time)
    summed = jnp.einsum("sxqjn,qsjz->xnz", section, depth_parts, precision=split_precision)
    summed = lax.optimization_barrier(summed.astype(jnp.bfloat16))
    grad_field = summed.reshape(x_local, channels, y_local, depth_time).transpose(1, 0, 2, 3)
    return (grad_field, grad_weight)


def solution(mesh):
    in_specs = (
        P(None, "gx", "gy", None),
        P(None, "gx", "gy", None),
        P(None, "gx", None, None, "gy", None),
    )
    out_specs = (P(None, "gx", "gy", None), P(None, "gx", None, None, "gy", None))
    return jax.shard_map(
        per_device, mesh=mesh, in_specs=in_specs, out_specs=out_specs, check_vma=False
    )
```

```python
import math

import jax
import jax.numpy as jnp
from jax import lax
from jax.sharding import PartitionSpec as P

MX = 12
MY = 12
MZ = 12
MT = 8
Z = 64
T_SIZE = 16
KX = 24
KY = 24
M = 192


exact_precision = lax.Precision.HIGHEST
split_precision = lax.Precision.HIGH
lead_contract = (((0,), (0,)), ((), ()))
tail_contract = (((1,), (1,)), ((), ()))


def signed_freqs(count, half_count):
    ladder = lax.iota(jnp.int32, count)
    return jnp.where(ladder < half_count, ladder, ladder - 2 * half_count)


def pair_table(frequencies, length):
    places = lax.iota(jnp.int32, length)
    residue = jnp.remainder(frequencies[:, None] * places[None, :], length)
    phases = residue.astype(jnp.float32) * (2.0 * math.pi / length)
    cosine = jnp.cos(phases) / math.sqrt(length)
    sines = jnp.sin(phases) / math.sqrt(length)
    return jnp.stack([jnp.stack([cosine, sines]), jnp.stack([-sines, cosine])])


def depth_rows_table():
    cell_ids = lax.iota(jnp.int32, Z * T_SIZE)
    depth_index = cell_ids // T_SIZE
    time_index = cell_ids % T_SIZE
    mode_ids = lax.iota(jnp.int32, M)
    depth_freq = mode_ids // MT
    depth_freq = jnp.where(depth_freq < MZ, depth_freq, depth_freq - 2 * MZ)
    time_freq = mode_ids % MT
    residue = jnp.remainder(
        depth_freq[:, None] * depth_index[None, :] * T_SIZE
        + time_freq[:, None] * time_index[None, :] * Z,
        Z * T_SIZE,
    )
    phases = residue.astype(jnp.float32) * (2.0 * math.pi / (Z * T_SIZE))
    factor = 1.0 / math.sqrt(Z * T_SIZE)
    return jnp.stack([jnp.cos(phases) * factor, -jnp.sin(phases) * factor])


def split_table(table):
    leading = table.astype(jnp.bfloat16)
    residual_part = (table - lax.optimization_barrier(leading).astype(jnp.float32)).astype(
        jnp.bfloat16
    )
    return (leading, residual_part)


def per_device(field_in, cotangent, spec_weight):
    channels, x_local, y_local, depth_time = field_in.shape
    x_groups = lax.axis_size("gx")
    x_count = x_local * x_groups
    y_count = y_local * lax.axis_size("gy")
    mode_local = M // x_groups
    x_table = pair_table(signed_freqs(KX, MX), x_count)
    x_blocks = x_table.reshape(2, 2, KX, x_groups, x_local)
    y_table = pair_table(signed_freqs(KY, MY), y_count)
    depth_modes = depth_rows_table()
    depth_flat = depth_modes.reshape(2 * M, depth_time)
    chunk_rows = depth_modes.reshape(2, x_groups, mode_local, depth_time).transpose(1, 0, 2, 3)
    depth_lead, depth_tail = split_table(chunk_rows.reshape(2 * M, depth_time))
    y_parts = lax.axis_size("gy")
    kx_local = KX // y_parts
    y_split = y_table.reshape(2, 2, KY, y_parts, y_local)

    def depth_forward(flat_rows):
        first = lax.dot_general(
            depth_lead, flat_rows, tail_contract, preferred_element_type=jnp.float32
        )
        return first + lax.dot_general(
            depth_tail, flat_rows, tail_contract, preferred_element_type=jnp.float32
        )

    def field_modes(field):
        slabs = [
            depth_forward(field[:, plane].reshape(channels * y_local, depth_time)).reshape(
                x_groups, 2 * mode_local, channels * y_local
            )
            for plane in range(x_local)
        ]
        spectra = jnp.stack(slabs, axis=1).reshape(
            x_groups, x_local, 2, mode_local, channels * y_local
        )
        section = lax.all_to_all(spectra, "gx", split_axis=0, concat_axis=0, tiled=True)
        summed_x = jnp.einsum("pqkbx,bxqjn->pkjn", x_blocks, section, precision=split_precision)
        summed_x = summed_x.reshape(2, y_parts, kx_local, mode_local, channels * y_local)
        summed_x = summed_x.transpose(1, 0, 2, 3, 4)
        gathered = lax.all_to_all(summed_x, "gy", split_axis=0, concat_axis=0, tiled=True)
        gathered = gathered.reshape(gathered.shape[:4] + (channels, y_local))
        return jnp.einsum("pqksy,sqajcy->pjcak", y_split, gathered, precision=split_precision)

    at_modes = jnp.stack([field_modes(field_in), field_modes(cotangent)])
    mode_ids = lax.axis_index("gx") * mode_local + lax.iota(jnp.int32, mode_local)
    doubling = jnp.where(mode_ids % MT == 0, 1.0, 2.0).astype(jnp.float32)[:, None, None, None]
    field_real = at_modes[0, 0]
    field_imag = at_modes[0, 1]
    dual_real = at_modes[1, 0] * doubling
    dual_imag = at_modes[1, 1] * doubling
    grad_real = (
        field_real[:, :, None] * dual_real[:, None] + field_imag[:, :, None] * dual_imag[:, None]
    )
    grad_imag = (
        field_real[:, :, None] * dual_imag[:, None] - field_imag[:, :, None] * dual_real[:, None]
    )
    grad_weight = jnp.stack([grad_real, grad_imag])
    back_real = jnp.sum(
        spec_weight[0] * dual_real[:, None] + spec_weight[1] * dual_imag[:, None], axis=2
    )
    back_imag = jnp.sum(
        spec_weight[0] * dual_imag[:, None] - spec_weight[1] * dual_real[:, None], axis=2
    )
    backward = jnp.stack([back_real, back_imag])
    y_parts = lax.axis_size("gy")
    y_chunks = y_table.reshape(2, 2, KY, y_parts, y_local)
    spread = jnp.einsum("qpkdy,qjcak->dpajcy", y_chunks, backward, precision=split_precision)
    spread = spread.reshape(spread.shape[:4] + (channels * y_local,))
    y_done = lax.all_to_all(spread, "gy", split_axis=0, concat_axis=0, tiled=True)
    x_inverse = x_table.reshape(2, 2, y_parts, KX // y_parts, x_groups, x_local)
    x_spread = jnp.einsum("pqsabx,spajn->bxqjn", x_inverse, y_done, precision=split_precision)
    section = lax.all_to_all(x_spread, "gx", split_axis=0, concat_axis=0, tiled=True)
    depth_parts = depth_flat.reshape(2, x_groups, mode_local, depth_time)
    summed = jnp.einsum("sxqjn,qsjz->xnz", section, depth_parts, precision=split_precision)
    summed = lax.optimization_barrier(summed.astype(jnp.bfloat16))
    grad_field = summed.reshape(x_local, channels, y_local, depth_time).transpose(1, 0, 2, 3)
    return (grad_field, grad_weight)


def solution(mesh):
    in_specs = (
        P(None, "gx", "gy", None),
        P(None, "gx", "gy", None),
        P(None, "gx", None, None, "gy", None),
    )
    out_specs = (P(None, "gx", "gy", None), P(None, "gx", None, None, "gy", None))
    return jax.shard_map(
        per_device, mesh=mesh, in_specs=in_specs, out_specs=out_specs, check_vma=False
    )
```

```python
import math

import jax
import jax.numpy as jnp
from jax import lax
from jax.sharding import PartitionSpec as P

MX = 12
MY = 12
MZ = 12
MT = 8
Z = 64
T_SIZE = 16
KX = 24
KY = 24
M = 192


exact_precision = lax.Precision.HIGHEST
split_precision = lax.Precision.HIGH
lead_contract = (((0,), (0,)), ((), ()))
tail_contract = (((1,), (1,)), ((), ()))


def signed_freqs(count, half_count):
    ladder = lax.iota(jnp.int32, count)
    return jnp.where(ladder < half_count, ladder, ladder - 2 * half_count)


def pair_table(frequencies, length):
    places = lax.iota(jnp.int32, length)
    residue = jnp.remainder(frequencies[:, None] * places[None, :], length)
    phases = residue.astype(jnp.float32) * (2.0 * math.pi / length)
    cosine = jnp.cos(phases) / math.sqrt(length)
    sines = jnp.sin(phases) / math.sqrt(length)
    return jnp.stack([jnp.stack([cosine, sines]), jnp.stack([-sines, cosine])])


def depth_rows_table():
    cell_ids = lax.iota(jnp.int32, Z * T_SIZE)
    depth_index = cell_ids // T_SIZE
    time_index = cell_ids % T_SIZE
    mode_ids = lax.iota(jnp.int32, M)
    depth_freq = mode_ids // MT
    depth_freq = jnp.where(depth_freq < MZ, depth_freq, depth_freq - 2 * MZ)
    time_freq = mode_ids % MT
    residue = jnp.remainder(
        depth_freq[:, None] * depth_index[None, :] * T_SIZE
        + time_freq[:, None] * time_index[None, :] * Z,
        Z * T_SIZE,
    )
    phases = residue.astype(jnp.float32) * (2.0 * math.pi / (Z * T_SIZE))
    factor = 1.0 / math.sqrt(Z * T_SIZE)
    return jnp.stack([jnp.cos(phases) * factor, -jnp.sin(phases) * factor])


def split_table(table):
    leading = table.astype(jnp.bfloat16)
    residual_part = (table - lax.optimization_barrier(leading).astype(jnp.float32)).astype(
        jnp.bfloat16
    )
    return (leading, residual_part)


def per_device(field_in, cotangent, spec_weight):
    channels, x_local, y_local, depth_time = field_in.shape
    x_groups = lax.axis_size("gx")
    x_count = x_local * x_groups
    y_count = y_local * lax.axis_size("gy")
    mode_local = M // x_groups
    x_table = pair_table(signed_freqs(KX, MX), x_count)
    x_blocks = x_table.reshape(2, 2, KX, x_groups, x_local)
    y_table = pair_table(signed_freqs(KY, MY), y_count)
    depth_modes = depth_rows_table()
    depth_flat = depth_modes.reshape(2 * M, depth_time)
    chunk_rows = depth_modes.reshape(2, x_groups, mode_local, depth_time).transpose(1, 0, 2, 3)
    depth_lead, depth_tail = split_table(chunk_rows.reshape(2 * M, depth_time))
    y_parts = lax.axis_size("gy")
    kx_local = KX // y_parts
    y_split = y_table.reshape(2, 2, KY, y_parts, y_local)

    def depth_forward(flat_rows):
        first = lax.dot_general(
            depth_lead, flat_rows, tail_contract, preferred_element_type=jnp.float32
        )
        return first + lax.dot_general(
            depth_tail, flat_rows, tail_contract, preferred_element_type=jnp.float32
        )

    def field_modes(field):
        slabs = [
            depth_forward(field[:, plane].reshape(channels * y_local, depth_time)).reshape(
                x_groups, 2 * mode_local, channels * y_local
            )
            for plane in range(x_local)
        ]
        spectra = jnp.stack(slabs, axis=1).reshape(
            x_groups, x_local, 2, mode_local, channels * y_local
        )
        section = lax.all_to_all(spectra, "gx", split_axis=0, concat_axis=0, tiled=True)
        summed_x = jnp.einsum("pqkbx,bxqjn->pkjn", x_blocks, section, precision=split_precision)
        summed_x = summed_x.reshape(2, y_parts, kx_local, mode_local, channels * y_local)
        summed_x = summed_x.transpose(1, 0, 2, 3, 4)
        gathered = lax.all_to_all(summed_x, "gy", split_axis=0, concat_axis=0, tiled=True)
        gathered = gathered.reshape(gathered.shape[:4] + (channels, y_local))
        return jnp.einsum("pqksy,sqajcy->pjcak", y_split, gathered, precision=split_precision)

    dual_modes = field_modes(cotangent)
    field_spectrum = field_modes(field_in)
    mode_ids = lax.axis_index("gx") * mode_local + lax.iota(jnp.int32, mode_local)
    doubling = jnp.where(mode_ids % MT == 0, 1.0, 2.0).astype(jnp.float32)[:, None, None, None]
    field_real = field_spectrum[0]
    field_imag = field_spectrum[1]
    dual_real = dual_modes[0] * doubling
    dual_imag = dual_modes[1] * doubling
    left = jnp.stack([field_real, field_real])[:, :, :, None]
    left_swap = jnp.stack([field_imag, -field_imag])[:, :, :, None]
    right = jnp.stack([dual_real, dual_imag])[:, :, None]
    right_swap = jnp.stack([dual_imag, dual_real])[:, :, None]
    grad_weight = left * right + left_swap * right_swap
    back_real = spec_weight[0][:, :, 0] * dual_real[:, :1] + spec_weight[1][:, :, 0] * dual_imag[:, :1]
    back_imag = spec_weight[0][:, :, 0] * dual_imag[:, :1] - spec_weight[1][:, :, 0] * dual_real[:, :1]
    for out_channel in range(1, channels):
        weight_real = spec_weight[0][:, :, out_channel]
        weight_imag = spec_weight[1][:, :, out_channel]
        dual_r = dual_real[:, out_channel : out_channel + 1]
        dual_i = dual_imag[:, out_channel : out_channel + 1]
        back_real = back_real + (weight_real * dual_r + weight_imag * dual_i)
        back_imag = back_imag + (weight_real * dual_i - weight_imag * dual_r)
    backward = jnp.stack([back_real, back_imag])
    y_parts = lax.axis_size("gy")
    y_chunks = y_table.reshape(2, 2, KY, y_parts, y_local)
    spread = jnp.einsum("qpkdy,qjcak->dpajcy", y_chunks, backward, precision=split_precision)
    spread = spread.reshape(spread.shape[:4] + (channels * y_local,))
    y_done = lax.all_to_all(spread, "gy", split_axis=0, concat_axis=0, tiled=True)
    x_inverse = x_table.reshape(2, 2, y_parts, KX // y_parts, x_groups, x_local)
    x_spread = jnp.einsum("pqsabx,spajn->bxqjn", x_inverse, y_done, precision=split_precision)
    section = lax.all_to_all(x_spread, "gx", split_axis=0, concat_axis=0, tiled=True)
    depth_parts = depth_flat.reshape(2, x_groups, mode_local, depth_time)
    summed = jnp.einsum("sxqjn,qsjz->xnz", section, depth_parts, precision=split_precision)
    summed = lax.optimization_barrier(summed.astype(jnp.bfloat16))
    grad_field = summed.reshape(x_local, channels, y_local, depth_time).transpose(1, 0, 2, 3)
    return (grad_field, grad_weight)


def solution(mesh):
    in_specs = (
        P(None, "gx", "gy", None),
        P(None, "gx", "gy", None),
        P(None, "gx", None, None, "gy", None),
    )
    out_specs = (P(None, "gx", "gy", None), P(None, "gx", None, None, "gy", None))
    return jax.shard_map(
        per_device, mesh=mesh, in_specs=in_specs, out_specs=out_specs, check_vma=False
    )
```

```python
import math

import jax
import jax.numpy as jnp
from jax import lax
from jax.sharding import PartitionSpec as P

MX = 12
MY = 12
MZ = 12
MT = 8
Z = 64
T_SIZE = 16
KX = 24
KY = 24
M = 192


exact_precision = lax.Precision.HIGHEST
split_precision = lax.Precision.HIGH
lead_contract = (((0,), (0,)), ((), ()))
tail_contract = (((1,), (1,)), ((), ()))


def signed_freqs(count, half_count):
    ladder = lax.iota(jnp.int32, count)
    return jnp.where(ladder < half_count, ladder, ladder - 2 * half_count)


def pair_table(frequencies, length):
    places = lax.iota(jnp.int32, length)
    residue = jnp.remainder(frequencies[:, None] * places[None, :], length)
    phases = residue.astype(jnp.float32) * (2.0 * math.pi / length)
    cosine = jnp.cos(phases) / math.sqrt(length)
    sines = jnp.sin(phases) / math.sqrt(length)
    return jnp.stack([jnp.stack([cosine, sines]), jnp.stack([-sines, cosine])])


def depth_rows_table():
    cell_ids = lax.iota(jnp.int32, Z * T_SIZE)
    depth_index = cell_ids // T_SIZE
    time_index = cell_ids % T_SIZE
    mode_ids = lax.iota(jnp.int32, M)
    depth_freq = mode_ids // MT
    depth_freq = jnp.where(depth_freq < MZ, depth_freq, depth_freq - 2 * MZ)
    time_freq = mode_ids % MT
    residue = jnp.remainder(
        depth_freq[:, None] * depth_index[None, :] * T_SIZE
        + time_freq[:, None] * time_index[None, :] * Z,
        Z * T_SIZE,
    )
    phases = residue.astype(jnp.float32) * (2.0 * math.pi / (Z * T_SIZE))
    factor = 1.0 / math.sqrt(Z * T_SIZE)
    return jnp.stack([jnp.cos(phases) * factor, -jnp.sin(phases) * factor])


def split_table(table):
    leading = table.astype(jnp.bfloat16)
    residual_part = (table - lax.optimization_barrier(leading).astype(jnp.float32)).astype(
        jnp.bfloat16
    )
    return (leading, residual_part)


def per_device(field_in, cotangent, spec_weight):
    channels, x_local, y_local, depth_time = field_in.shape
    x_groups = lax.axis_size("gx")
    x_count = x_local * x_groups
    y_count = y_local * lax.axis_size("gy")
    mode_local = M // x_groups
    x_table = pair_table(signed_freqs(KX, MX), x_count)
    x_blocks = x_table.reshape(2, 2, KX, x_groups, x_local)
    y_table = pair_table(signed_freqs(KY, MY), y_count)
    depth_modes = depth_rows_table()
    depth_flat = depth_modes.reshape(2 * M, depth_time)
    chunk_rows = depth_modes.reshape(2, x_groups, mode_local, depth_time).transpose(1, 0, 2, 3)
    depth_lead, depth_tail = split_table(chunk_rows.reshape(2 * M, depth_time))
    y_parts = lax.axis_size("gy")
    kx_local = KX // y_parts
    y_split = y_table.reshape(2, 2, KY, y_parts, y_local)

    def depth_forward(planes):
        contract = (((1,), (2,)), ((), ()))
        first = lax.dot_general(depth_lead, planes, contract, preferred_element_type=jnp.float32)
        return first + lax.dot_general(
            depth_tail, planes, contract, preferred_element_type=jnp.float32
        )

    def field_modes(field):
        planes = field.transpose(1, 0, 2, 3).reshape(x_local, channels * y_local, depth_time)
        spectra = depth_forward(planes).reshape(
            x_groups, 2, mode_local, x_local, channels * y_local
        )
        section = lax.all_to_all(spectra, "gx", split_axis=0, concat_axis=0, tiled=True)
        summed_x = jnp.einsum("pqkbx,bqjxn->pkjn", x_blocks, section, precision=split_precision)
        summed_x = summed_x.reshape(2, y_parts, kx_local, mode_local, channels * y_local)
        summed_x = summed_x.transpose(1, 0, 2, 3, 4)
        gathered = lax.all_to_all(summed_x, "gy", split_axis=0, concat_axis=0, tiled=True)
        gathered = gathered.reshape(gathered.shape[:4] + (channels, y_local))
        return jnp.einsum("pqksy,sqajcy->pjcak", y_split, gathered, precision=split_precision)

    dual_modes = field_modes(cotangent)
    field_spectrum = field_modes(field_in)
    mode_ids = lax.axis_index("gx") * mode_local + lax.iota(jnp.int32, mode_local)
    doubling = jnp.where(mode_ids % MT == 0, 1.0, 2.0).astype(jnp.float32)[:, None, None, None]
    field_real = field_spectrum[0]
    field_imag = field_spectrum[1]
    dual_real = dual_modes[0] * doubling
    dual_imag = dual_modes[1] * doubling
    left = jnp.stack([field_real, field_real])[:, :, :, None]
    left_swap = jnp.stack([field_imag, -field_imag])[:, :, :, None]
    right = jnp.stack([dual_real, dual_imag])[:, :, None]
    right_swap = jnp.stack([dual_imag, dual_real])[:, :, None]
    grad_weight = left * right + left_swap * right_swap
    back_real = spec_weight[0][:, :, 0] * dual_real[:, :1] + spec_weight[1][:, :, 0] * dual_imag[:, :1]
    back_imag = spec_weight[0][:, :, 0] * dual_imag[:, :1] - spec_weight[1][:, :, 0] * dual_real[:, :1]
    for out_channel in range(1, channels):
        weight_real = spec_weight[0][:, :, out_channel]
        weight_imag = spec_weight[1][:, :, out_channel]
        dual_r = dual_real[:, out_channel : out_channel + 1]
        dual_i = dual_imag[:, out_channel : out_channel + 1]
        back_real = back_real + (weight_real * dual_r + weight_imag * dual_i)
        back_imag = back_imag + (weight_real * dual_i - weight_imag * dual_r)
    backward = jnp.stack([back_real, back_imag])
    y_parts = lax.axis_size("gy")
    y_chunks = y_table.reshape(2, 2, KY, y_parts, y_local)
    spread = jnp.einsum("qpkdy,qjcak->dpajcy", y_chunks, backward, precision=split_precision)
    spread = spread.reshape(spread.shape[:4] + (channels * y_local,))
    y_done = lax.all_to_all(spread, "gy", split_axis=0, concat_axis=0, tiled=True)
    x_inverse = x_table.reshape(2, 2, y_parts, KX // y_parts, x_groups, x_local)
    x_spread = jnp.einsum("pqsabx,spajn->bxqjn", x_inverse, y_done, precision=split_precision)
    section = lax.all_to_all(x_spread, "gx", split_axis=0, concat_axis=0, tiled=True)
    depth_parts = depth_flat.reshape(2, x_groups, mode_local, depth_time)
    summed = jnp.einsum("sxqjn,qsjz->xnz", section, depth_parts, precision=split_precision)
    summed = lax.optimization_barrier(summed.astype(jnp.bfloat16))
    grad_field = summed.reshape(x_local, channels, y_local, depth_time).transpose(1, 0, 2, 3)
    return (grad_field, grad_weight)


def solution(mesh):
    in_specs = (
        P(None, "gx", "gy", None),
        P(None, "gx", "gy", None),
        P(None, "gx", None, None, "gy", None),
    )
    out_specs = (P(None, "gx", "gy", None), P(None, "gx", None, None, "gy", None))
    return jax.shard_map(
        per_device, mesh=mesh, in_specs=in_specs, out_specs=out_specs, check_vma=False
    )
```

```python
import math

import jax
import jax.numpy as jnp
from jax import lax
from jax.sharding import PartitionSpec as P

MX = 12
MY = 12
MZ = 12
MT = 8
Z = 64
T_SIZE = 16
KX = 24
KY = 24
M = 192


exact_precision = lax.Precision.HIGHEST
split_precision = lax.Precision.HIGH
lead_contract = (((0,), (0,)), ((), ()))
tail_contract = (((1,), (1,)), ((), ()))


def signed_freqs(count, half_count):
    ladder = lax.iota(jnp.int32, count)
    return jnp.where(ladder < half_count, ladder, ladder - 2 * half_count)


def pair_table(frequencies, length):
    places = lax.iota(jnp.int32, length)
    residue = jnp.remainder(frequencies[:, None] * places[None, :], length)
    phases = residue.astype(jnp.float32) * (2.0 * math.pi / length)
    cosine = jnp.cos(phases) / math.sqrt(length)
    sines = jnp.sin(phases) / math.sqrt(length)
    return jnp.stack([jnp.stack([cosine, sines]), jnp.stack([-sines, cosine])])


def depth_rows_table():
    cell_ids = lax.iota(jnp.int32, Z * T_SIZE)
    depth_index = cell_ids // T_SIZE
    time_index = cell_ids % T_SIZE
    mode_ids = lax.iota(jnp.int32, M)
    depth_freq = mode_ids // MT
    depth_freq = jnp.where(depth_freq < MZ, depth_freq, depth_freq - 2 * MZ)
    time_freq = mode_ids % MT
    residue = jnp.remainder(
        depth_freq[:, None] * depth_index[None, :] * T_SIZE
        + time_freq[:, None] * time_index[None, :] * Z,
        Z * T_SIZE,
    )
    phases = residue.astype(jnp.float32) * (2.0 * math.pi / (Z * T_SIZE))
    factor = 1.0 / math.sqrt(Z * T_SIZE)
    return jnp.stack([jnp.cos(phases) * factor, -jnp.sin(phases) * factor])


def split_table(table):
    leading = table.astype(jnp.bfloat16)
    residual_part = (table - lax.optimization_barrier(leading).astype(jnp.float32)).astype(
        jnp.bfloat16
    )
    return (leading, residual_part)


def per_device(field_in, cotangent, spec_weight):
    channels, x_local, y_local, depth_time = field_in.shape
    x_groups = lax.axis_size("gx")
    x_count = x_local * x_groups
    y_count = y_local * lax.axis_size("gy")
    mode_local = M // x_groups
    x_table = pair_table(signed_freqs(KX, MX), x_count)
    x_blocks = x_table.reshape(2, 2, KX, x_groups, x_local)
    y_table = pair_table(signed_freqs(KY, MY), y_count)
    depth_modes = depth_rows_table()
    depth_flat = depth_modes.reshape(2 * M, depth_time)
    chunk_rows = depth_modes.reshape(2, x_groups, mode_local, depth_time).transpose(1, 0, 2, 3)
    depth_lead, depth_tail = split_table(chunk_rows.reshape(2 * M, depth_time))
    y_parts = lax.axis_size("gy")
    kx_local = KX // y_parts
    y_split = y_table.reshape(2, 2, KY, y_parts, y_local)

    def depth_forward(planes):
        contract = (((1,), (2,)), ((), ()))
        first = lax.dot_general(depth_lead, planes, contract, preferred_element_type=jnp.float32)
        return first + lax.dot_general(
            depth_tail, planes, contract, preferred_element_type=jnp.float32
        )

    channel_eye = jnp.eye(channels, dtype=jnp.float32)
    y_near = lax.dynamic_index_in_dim(y_split, lax.axis_index("gy"), axis=3, keepdims=False)
    y_kron = jnp.einsum("cd,pqky->qcypdk", channel_eye, y_near).reshape(
        2, channels * y_local, 2, channels * KY
    )

    def field_modes(field):
        planes = field.transpose(1, 0, 2, 3).reshape(x_local, channels * y_local, depth_time)
        spectra = depth_forward(planes).reshape(
            x_groups, 2, mode_local, x_local, channels * y_local
        )
        partial_y = lax.dot_general(
            spectra, y_kron, (((1, 4), (0, 1)), ((), ())), precision=split_precision
        )
        section = lax.all_to_all(partial_y, "gx", split_axis=0, concat_axis=0, tiled=True)
        summed_x = jnp.einsum("pqkbx,bjxqn->pkjn", x_blocks, section, precision=split_precision)
        summed_x = summed_x.reshape(2, y_parts, kx_local, mode_local, channels * KY)
        summed_x = summed_x.transpose(1, 0, 2, 3, 4)
        gathered = lax.all_to_all(summed_x, "gy", split_axis=0, concat_axis=0, tiled=True)
        summed_y = jnp.sum(gathered, axis=0).reshape(2, kx_local, mode_local, channels, KY)
        return summed_y.transpose(0, 2, 3, 1, 4)

    dual_modes = field_modes(cotangent)
    field_spectrum = field_modes(field_in)
    mode_ids = lax.axis_index("gx") * mode_local + lax.iota(jnp.int32, mode_local)
    doubling = jnp.where(mode_ids % MT == 0, 1.0, 2.0).astype(jnp.float32)[:, None, None, None]
    field_real = field_spectrum[0]
    field_imag = field_spectrum[1]
    dual_real = dual_modes[0] * doubling
    dual_imag = dual_modes[1] * doubling
    left = jnp.stack([field_real, field_real])[:, :, :, None]
    left_swap = jnp.stack([field_imag, -field_imag])[:, :, :, None]
    right = jnp.stack([dual_real, dual_imag])[:, :, None]
    right_swap = jnp.stack([dual_imag, dual_real])[:, :, None]
    grad_weight = left * right + left_swap * right_swap
    back_real = spec_weight[0][:, :, 0] * dual_real[:, :1] + spec_weight[1][:, :, 0] * dual_imag[:, :1]
    back_imag = spec_weight[0][:, :, 0] * dual_imag[:, :1] - spec_weight[1][:, :, 0] * dual_real[:, :1]
    for out_channel in range(1, channels):
        weight_real = spec_weight[0][:, :, out_channel]
        weight_imag = spec_weight[1][:, :, out_channel]
        dual_r = dual_real[:, out_channel : out_channel + 1]
        dual_i = dual_imag[:, out_channel : out_channel + 1]
        back_real = back_real + (weight_real * dual_r + weight_imag * dual_i)
        back_imag = back_imag + (weight_real * dual_i - weight_imag * dual_r)
    backward = jnp.stack([back_real, back_imag])
    y_parts = lax.axis_size("gy")
    y_chunks = y_table.reshape(2, 2, KY, y_parts, y_local)
    spread = jnp.einsum("qpkdy,qjcak->dpajcy", y_chunks, backward, precision=split_precision)
    spread = spread.reshape(spread.shape[:4] + (channels * y_local,))
    y_done = lax.all_to_all(spread, "gy", split_axis=0, concat_axis=0, tiled=True)
    x_inverse = x_table.reshape(2, 2, y_parts, KX // y_parts, x_groups, x_local)
    x_spread = jnp.einsum("pqsabx,spajn->bxqjn", x_inverse, y_done, precision=split_precision)
    section = lax.all_to_all(x_spread, "gx", split_axis=0, concat_axis=0, tiled=True)
    depth_parts = depth_flat.reshape(2, x_groups, mode_local, depth_time)
    summed = jnp.einsum("sxqjn,qsjz->xnz", section, depth_parts, precision=split_precision)
    summed = lax.optimization_barrier(summed.astype(jnp.bfloat16))
    grad_field = summed.reshape(x_local, channels, y_local, depth_time).transpose(1, 0, 2, 3)
    return (grad_field, grad_weight)


def solution(mesh):
    in_specs = (
        P(None, "gx", "gy", None),
        P(None, "gx", "gy", None),
        P(None, "gx", None, None, "gy", None),
    )
    out_specs = (P(None, "gx", "gy", None), P(None, "gx", None, None, "gy", None))
    return jax.shard_map(
        per_device, mesh=mesh, in_specs=in_specs, out_specs=out_specs, check_vma=False
    )
```

```python
import math

import jax
import jax.numpy as jnp
from jax import lax
from jax.sharding import PartitionSpec as P

MX = 12
MY = 12
MZ = 12
MT = 8
Z = 64
T_SIZE = 16
KX = 24
KY = 24
M = 192


exact_precision = lax.Precision.HIGHEST
split_precision = lax.Precision.HIGH
lead_contract = (((0,), (0,)), ((), ()))
tail_contract = (((1,), (1,)), ((), ()))


def signed_freqs(count, half_count):
    ladder = lax.iota(jnp.int32, count)
    return jnp.where(ladder < half_count, ladder, ladder - 2 * half_count)


def pair_table(frequencies, length):
    places = lax.iota(jnp.int32, length)
    residue = jnp.remainder(frequencies[:, None] * places[None, :], length)
    phases = residue.astype(jnp.float32) * (2.0 * math.pi / length)
    cosine = jnp.cos(phases) / math.sqrt(length)
    sines = jnp.sin(phases) / math.sqrt(length)
    return jnp.stack([jnp.stack([cosine, sines]), jnp.stack([-sines, cosine])])


def depth_rows_table():
    cell_ids = lax.iota(jnp.int32, Z * T_SIZE)
    depth_index = cell_ids // T_SIZE
    time_index = cell_ids % T_SIZE
    mode_ids = lax.iota(jnp.int32, M)
    depth_freq = mode_ids // MT
    depth_freq = jnp.where(depth_freq < MZ, depth_freq, depth_freq - 2 * MZ)
    time_freq = mode_ids % MT
    residue = jnp.remainder(
        depth_freq[:, None] * depth_index[None, :] * T_SIZE
        + time_freq[:, None] * time_index[None, :] * Z,
        Z * T_SIZE,
    )
    phases = residue.astype(jnp.float32) * (2.0 * math.pi / (Z * T_SIZE))
    factor = 1.0 / math.sqrt(Z * T_SIZE)
    return jnp.stack([jnp.cos(phases) * factor, -jnp.sin(phases) * factor])


def split_table(table):
    leading = table.astype(jnp.bfloat16)
    residual_part = (table - lax.optimization_barrier(leading).astype(jnp.float32)).astype(
        jnp.bfloat16
    )
    return (leading, residual_part)


def per_device(field_in, cotangent, spec_weight):
    channels, x_local, y_local, depth_time = field_in.shape
    x_groups = lax.axis_size("gx")
    x_count = x_local * x_groups
    y_count = y_local * lax.axis_size("gy")
    mode_local = M // x_groups
    x_table = pair_table(signed_freqs(KX, MX), x_count)
    x_blocks = x_table.reshape(2, 2, KX, x_groups, x_local)
    y_table = pair_table(signed_freqs(KY, MY), y_count)
    depth_modes = depth_rows_table()
    depth_flat = depth_modes.reshape(2 * M, depth_time)
    chunk_rows = depth_modes.reshape(2, x_groups, mode_local, depth_time).transpose(1, 0, 2, 3)
    depth_lead, depth_tail = split_table(chunk_rows.reshape(2 * M, depth_time))
    y_parts = lax.axis_size("gy")
    kx_local = KX // y_parts
    y_split = y_table.reshape(2, 2, KY, y_parts, y_local)

    def depth_forward(planes):
        contract = (((1,), (2,)), ((), ()))
        first = lax.dot_general(depth_lead, planes, contract, preferred_element_type=jnp.float32)
        return first + lax.dot_general(
            depth_tail, planes, contract, preferred_element_type=jnp.float32
        )

    channel_eye = jnp.eye(channels, dtype=jnp.float32)
    y_near = lax.dynamic_index_in_dim(y_split, lax.axis_index("gy"), axis=3, keepdims=False)
    y_kron = jnp.einsum("cd,pqky->qcypdk", channel_eye, y_near).reshape(
        2, channels * y_local, 2, channels * KY
    )

    def field_modes(field):
        planes = field.transpose(1, 0, 2, 3).reshape(x_local, channels * y_local, depth_time)
        spectra = depth_forward(planes).reshape(
            x_groups, 2, mode_local, x_local, channels * y_local
        )
        partial_y = lax.dot_general(
            spectra, y_kron, (((1, 4), (0, 1)), ((), ())), precision=split_precision
        )
        section = lax.all_to_all(partial_y, "gx", split_axis=0, concat_axis=0, tiled=True)
        summed_x = jnp.einsum("pqkbx,bjxqn->pkjn", x_blocks, section, precision=split_precision)
        summed_x = summed_x.reshape(2, y_parts, kx_local, mode_local, channels * KY)
        summed_x = summed_x.transpose(1, 0, 2, 3, 4)
        gathered = lax.all_to_all(summed_x, "gy", split_axis=0, concat_axis=0, tiled=True)
        summed_y = jnp.sum(gathered, axis=0).reshape(2, kx_local, mode_local, channels, KY)
        return summed_y.transpose(0, 2, 3, 1, 4)

    def full_modes(field):
        planes = field.transpose(1, 0, 2, 3).reshape(x_local, channels * y_local, depth_time)
        spectra = depth_forward(planes).reshape(
            x_groups, 2, mode_local, x_local, channels * y_local
        )
        section = lax.all_to_all(spectra, "gx", split_axis=0, concat_axis=0, tiled=True)
        summed_x = jnp.einsum("pqkbx,bqjxn->pkjn", x_blocks, section, precision=split_precision)
        summed_x = summed_x.reshape(2, y_parts, kx_local, mode_local, channels * y_local)
        summed_x = summed_x.transpose(1, 0, 2, 3, 4)
        gathered = lax.all_to_all(summed_x, "gy", split_axis=0, concat_axis=0, tiled=True)
        gathered = gathered.reshape(gathered.shape[:4] + (channels, y_local))
        return jnp.einsum("pqksy,sqajcy->pjcak", y_split, gathered, precision=split_precision)

    dual_modes = full_modes(cotangent)
    field_spectrum = field_modes(field_in)
    mode_ids = lax.axis_index("gx") * mode_local + lax.iota(jnp.int32, mode_local)
    doubling = jnp.where(mode_ids % MT == 0, 1.0, 2.0).astype(jnp.float32)[:, None, None, None]
    field_real = field_spectrum[0]
    field_imag = field_spectrum[1]
    dual_real = dual_modes[0] * doubling
    dual_imag = dual_modes[1] * doubling
    left = jnp.stack([field_real, field_real])[:, :, :, None]
    left_swap = jnp.stack([field_imag, -field_imag])[:, :, :, None]
    right = jnp.stack([dual_real, dual_imag])[:, :, None]
    right_swap = jnp.stack([dual_imag, dual_real])[:, :, None]
    grad_weight = left * right + left_swap * right_swap
    back_real = spec_weight[0][:, :, 0] * dual_real[:, :1] + spec_weight[1][:, :, 0] * dual_imag[:, :1]
    back_imag = spec_weight[0][:, :, 0] * dual_imag[:, :1] - spec_weight[1][:, :, 0] * dual_real[:, :1]
    for out_channel in range(1, channels):
        weight_real = spec_weight[0][:, :, out_channel]
        weight_imag = spec_weight[1][:, :, out_channel]
        dual_r = dual_real[:, out_channel : out_channel + 1]
        dual_i = dual_imag[:, out_channel : out_channel + 1]
        back_real = back_real + (weight_real * dual_r + weight_imag * dual_i)
        back_imag = back_imag + (weight_real * dual_i - weight_imag * dual_r)
    backward = jnp.stack([back_real, back_imag])
    y_parts = lax.axis_size("gy")
    y_chunks = y_table.reshape(2, 2, KY, y_parts, y_local)
    spread = jnp.einsum("qpkdy,qjcak->dpajcy", y_chunks, backward, precision=split_precision)
    spread = spread.reshape(spread.shape[:4] + (channels * y_local,))
    y_done = lax.all_to_all(spread, "gy", split_axis=0, concat_axis=0, tiled=True)
    x_inverse = x_table.reshape(2, 2, y_parts, KX // y_parts, x_groups, x_local)
    x_spread = jnp.einsum("pqsabx,spajn->bxqjn", x_inverse, y_done, precision=split_precision)
    section = lax.all_to_all(x_spread, "gx", split_axis=0, concat_axis=0, tiled=True)
    depth_parts = depth_flat.reshape(2, x_groups, mode_local, depth_time)
    summed = jnp.einsum("sxqjn,qsjz->xnz", section, depth_parts, precision=split_precision)
    summed = lax.optimization_barrier(summed.astype(jnp.bfloat16))
    grad_field = summed.reshape(x_local, channels, y_local, depth_time).transpose(1, 0, 2, 3)
    return (grad_field, grad_weight)


def solution(mesh):
    in_specs = (
        P(None, "gx", "gy", None),
        P(None, "gx", "gy", None),
        P(None, "gx", None, None, "gy", None),
    )
    out_specs = (P(None, "gx", "gy", None), P(None, "gx", None, None, "gy", None))
    return jax.shard_map(
        per_device, mesh=mesh, in_specs=in_specs, out_specs=out_specs, check_vma=False
    )
```

```python
import math

import jax
import jax.numpy as jnp
from jax import lax
from jax.sharding import PartitionSpec as P

MX = 12
MY = 12
MZ = 12
MT = 8
Z = 64
T_SIZE = 16
KX = 24
KY = 24
M = 192


exact_precision = lax.Precision.HIGHEST
split_precision = lax.Precision.HIGH
lead_contract = (((0,), (0,)), ((), ()))
tail_contract = (((1,), (1,)), ((), ()))


def signed_freqs(count, half_count):
    ladder = lax.iota(jnp.int32, count)
    return jnp.where(ladder < half_count, ladder, ladder - 2 * half_count)


def pair_table(frequencies, length):
    places = lax.iota(jnp.int32, length)
    residue = jnp.remainder(frequencies[:, None] * places[None, :], length)
    phases = residue.astype(jnp.float32) * (2.0 * math.pi / length)
    cosine = jnp.cos(phases) / math.sqrt(length)
    sines = jnp.sin(phases) / math.sqrt(length)
    return jnp.stack([jnp.stack([cosine, sines]), jnp.stack([-sines, cosine])])


def depth_rows_table():
    cell_ids = lax.iota(jnp.int32, Z * T_SIZE)
    depth_index = cell_ids // T_SIZE
    time_index = cell_ids % T_SIZE
    mode_ids = lax.iota(jnp.int32, M)
    depth_freq = mode_ids // MT
    depth_freq = jnp.where(depth_freq < MZ, depth_freq, depth_freq - 2 * MZ)
    time_freq = mode_ids % MT
    residue = jnp.remainder(
        depth_freq[:, None] * depth_index[None, :] * T_SIZE
        + time_freq[:, None] * time_index[None, :] * Z,
        Z * T_SIZE,
    )
    phases = residue.astype(jnp.float32) * (2.0 * math.pi / (Z * T_SIZE))
    factor = 1.0 / math.sqrt(Z * T_SIZE)
    return jnp.stack([jnp.cos(phases) * factor, -jnp.sin(phases) * factor])


def split_table(table):
    leading = table.astype(jnp.bfloat16)
    residual_part = (table - lax.optimization_barrier(leading).astype(jnp.float32)).astype(
        jnp.bfloat16
    )
    return (leading, residual_part)


def per_device(field_in, cotangent, spec_weight):
    channels, x_local, y_local, depth_time = field_in.shape
    x_groups = lax.axis_size("gx")
    x_count = x_local * x_groups
    y_count = y_local * lax.axis_size("gy")
    mode_local = M // x_groups
    x_table = pair_table(signed_freqs(KX, MX), x_count)
    x_blocks = x_table.reshape(2, 2, KX, x_groups, x_local)
    y_table = pair_table(signed_freqs(KY, MY), y_count)
    depth_modes = depth_rows_table()
    depth_flat = depth_modes.reshape(2 * M, depth_time)
    chunk_rows = depth_modes.reshape(2, x_groups, mode_local, depth_time).transpose(1, 0, 2, 3)
    depth_lead, depth_tail = split_table(chunk_rows.reshape(2 * M, depth_time))
    y_parts = lax.axis_size("gy")
    kx_local = KX // y_parts
    y_split = y_table.reshape(2, 2, KY, y_parts, y_local)

    def depth_forward(planes):
        contract = (((1,), (2,)), ((), ()))
        first = lax.dot_general(depth_lead, planes, contract, preferred_element_type=jnp.float32)
        return first + lax.dot_general(
            depth_tail, planes, contract, preferred_element_type=jnp.float32
        )

    channel_eye = jnp.eye(channels, dtype=jnp.float32)
    y_near = lax.dynamic_index_in_dim(y_split, lax.axis_index("gy"), axis=3, keepdims=False)
    y_kron = jnp.einsum("cd,pqky->qcypdk", channel_eye, y_near).reshape(
        2, channels * y_local, 2, channels * KY
    )

    def field_modes(field):
        planes = field.transpose(1, 0, 2, 3).reshape(x_local, channels * y_local, depth_time)
        spectra = depth_forward(planes).reshape(
            x_groups, 2, mode_local, x_local, channels * y_local
        )
        partial_y = lax.dot_general(
            spectra, y_kron, (((1, 4), (0, 1)), ((), ())), precision=split_precision
        )
        section = lax.all_to_all(partial_y, "gx", split_axis=0, concat_axis=0, tiled=True)
        summed_x = jnp.einsum("pqkbx,bjxqn->pkjn", x_blocks, section, precision=split_precision)
        summed_x = summed_x.reshape(2, y_parts, kx_local, mode_local, channels * KY)
        summed_x = summed_x.transpose(1, 0, 2, 3, 4)
        gathered = lax.all_to_all(summed_x, "gy", split_axis=0, concat_axis=0, tiled=True)
        summed_y = jnp.sum(gathered, axis=0).reshape(2, kx_local, mode_local, channels, KY)
        return summed_y.transpose(0, 2, 3, 1, 4)

    def full_modes(field):
        planes = field.transpose(1, 0, 2, 3).reshape(x_local, channels * y_local, depth_time)
        spectra = depth_forward(planes).reshape(
            x_groups, 2, mode_local, x_local, channels * y_local
        )
        section = lax.all_to_all(spectra, "gx", split_axis=0, concat_axis=0, tiled=True)
        summed_x = jnp.einsum("pqkbx,bqjxn->pkjn", x_blocks, section, precision=split_precision)
        summed_x = summed_x.reshape(2, y_parts, kx_local, mode_local, channels * y_local)
        summed_x = summed_x.transpose(1, 0, 2, 3, 4)
        gathered = lax.all_to_all(summed_x, "gy", split_axis=0, concat_axis=0, tiled=True)
        gathered = gathered.reshape(gathered.shape[:4] + (channels, y_local))
        return jnp.einsum("pqksy,sqajcy->pjcak", y_split, gathered, precision=split_precision)

    dual_modes = full_modes(cotangent)
    field_spectrum = field_modes(field_in)
    mode_ids = lax.axis_index("gx") * mode_local + lax.iota(jnp.int32, mode_local)
    doubling = jnp.where(mode_ids % MT == 0, 1.0, 2.0).astype(jnp.float32)[:, None, None, None]
    field_real = field_spectrum[0]
    field_imag = field_spectrum[1]
    dual_real = dual_modes[0] * doubling
    dual_imag = dual_modes[1] * doubling
    left = jnp.stack([field_real, field_real])[:, :, :, None]
    left_swap = jnp.stack([field_imag, -field_imag])[:, :, :, None]
    right = jnp.stack([dual_real, dual_imag])[:, :, None]
    right_swap = jnp.stack([dual_imag, dual_real])[:, :, None]
    grad_weight = left * right + left_swap * right_swap
    back_real = spec_weight[0][:, :, 0] * dual_real[:, :1] + spec_weight[1][:, :, 0] * dual_imag[:, :1]
    back_imag = spec_weight[0][:, :, 0] * dual_imag[:, :1] - spec_weight[1][:, :, 0] * dual_real[:, :1]
    for out_channel in range(1, channels):
        weight_real = spec_weight[0][:, :, out_channel]
        weight_imag = spec_weight[1][:, :, out_channel]
        dual_r = dual_real[:, out_channel : out_channel + 1]
        dual_i = dual_imag[:, out_channel : out_channel + 1]
        back_real = back_real + (weight_real * dual_r + weight_imag * dual_i)
        back_imag = back_imag + (weight_real * dual_i - weight_imag * dual_r)
    backward = jnp.stack([back_real, back_imag])
    by_mode = backward.transpose(0, 3, 1, 2, 4).reshape(2, kx_local, mode_local, channels * KY)
    copies = jnp.broadcast_to(by_mode[None], (y_parts,) + by_mode.shape)
    y_done = lax.all_to_all(copies, "gy", split_axis=0, concat_axis=0, tiled=True)
    x_inverse = x_table.reshape(2, 2, y_parts, kx_local, x_groups, x_local)
    x_spread = jnp.einsum("pqsabx,spajn->bxqjn", x_inverse, y_done, precision=split_precision)
    section = lax.all_to_all(x_spread, "gx", split_axis=0, concat_axis=0, tiled=True)
    y_back = jnp.einsum("cd,qpky->qckpdy", channel_eye, y_near).reshape(
        2, channels * KY, 2, channels * y_local
    )
    rows = lax.dot_general(
        section, y_back, (((2, 4), (0, 1)), ((), ())), precision=split_precision
    )
    depth_parts = depth_flat.reshape(2, x_groups, mode_local, depth_time)
    summed = jnp.einsum("sxjpn,psjz->xnz", rows, depth_parts, precision=split_precision)
    summed = lax.optimization_barrier(summed.astype(jnp.bfloat16))
    grad_field = summed.reshape(x_local, channels, y_local, depth_time).transpose(1, 0, 2, 3)
    return (grad_field, grad_weight)


def solution(mesh):
    in_specs = (
        P(None, "gx", "gy", None),
        P(None, "gx", "gy", None),
        P(None, "gx", None, None, "gy", None),
    )
    out_specs = (P(None, "gx", "gy", None), P(None, "gx", None, None, "gy", None))
    return jax.shard_map(
        per_device, mesh=mesh, in_specs=in_specs, out_specs=out_specs, check_vma=False
    )
```

```python
import math

import jax
import jax.numpy as jnp
from jax import lax
from jax.sharding import PartitionSpec as P

MX = 12
MY = 12
MZ = 12
MT = 8
Z = 64
T_SIZE = 16
KX = 24
KY = 24
M = 192


split_precision = lax.Precision.HIGH


def signed_freqs(count, half_count):
    ladder = lax.iota(jnp.int32, count)
    return jnp.where(ladder < half_count, ladder, ladder - 2 * half_count)


def pair_table(frequencies, length):
    places = lax.iota(jnp.int32, length)
    residue = jnp.remainder(frequencies[:, None] * places[None, :], length)
    phases = residue.astype(jnp.float32) * (2.0 * math.pi / length)
    cosine = jnp.cos(phases) / math.sqrt(length)
    sines = jnp.sin(phases) / math.sqrt(length)
    return jnp.stack([jnp.stack([cosine, sines]), jnp.stack([-sines, cosine])])


def depth_rows_table():
    cell_ids = lax.iota(jnp.int32, Z * T_SIZE)
    depth_index = cell_ids // T_SIZE
    time_index = cell_ids % T_SIZE
    mode_ids = lax.iota(jnp.int32, M)
    depth_freq = mode_ids // MT
    depth_freq = jnp.where(depth_freq < MZ, depth_freq, depth_freq - 2 * MZ)
    time_freq = mode_ids % MT
    residue = jnp.remainder(
        depth_freq[:, None] * depth_index[None, :] * T_SIZE
        + time_freq[:, None] * time_index[None, :] * Z,
        Z * T_SIZE,
    )
    phases = residue.astype(jnp.float32) * (2.0 * math.pi / (Z * T_SIZE))
    factor = 1.0 / math.sqrt(Z * T_SIZE)
    return jnp.stack([jnp.cos(phases) * factor, -jnp.sin(phases) * factor])


def split_table(table):
    leading = table.astype(jnp.bfloat16)
    residual_part = (table - lax.optimization_barrier(leading).astype(jnp.float32)).astype(
        jnp.bfloat16
    )
    return (leading, residual_part)


def layer_body(field_in, cotangent, spec_weight):
    channels, x_local, y_local, depth_time = field_in.shape
    x_groups = lax.axis_size("gx")
    x_count = x_local * x_groups
    y_count = y_local * lax.axis_size("gy")
    mode_local = M // x_groups
    x_table = pair_table(signed_freqs(KX, MX), x_count)
    x_blocks = x_table.reshape(2, 2, KX, x_groups, x_local)
    y_table = pair_table(signed_freqs(KY, MY), y_count)
    depth_modes = depth_rows_table()
    depth_flat = depth_modes.reshape(2 * M, depth_time)
    chunk_rows = depth_modes.reshape(2, x_groups, mode_local, depth_time).transpose(1, 0, 2, 3)
    depth_lead, depth_tail = split_table(chunk_rows.reshape(2 * M, depth_time))
    y_parts = lax.axis_size("gy")
    kx_local = KX // y_parts
    y_split = y_table.reshape(2, 2, KY, y_parts, y_local)

    def depth_forward(planes):
        contract = (((1,), (2,)), ((), ()))
        first = lax.dot_general(depth_lead, planes, contract, preferred_element_type=jnp.float32)
        return first + lax.dot_general(
            depth_tail, planes, contract, preferred_element_type=jnp.float32
        )

    channel_eye = jnp.eye(channels, dtype=jnp.float32)
    y_near = lax.dynamic_index_in_dim(y_split, lax.axis_index("gy"), axis=3, keepdims=False)
    y_kron = jnp.einsum("cd,pqky->qcypdk", channel_eye, y_near).reshape(
        2, channels * y_local, 2, channels * KY
    )

    def field_modes(field):
        planes = field.transpose(1, 0, 2, 3).reshape(x_local, channels * y_local, depth_time)
        spectra = depth_forward(planes).reshape(
            x_groups, 2, mode_local, x_local, channels * y_local
        )
        partial_y = lax.dot_general(
            spectra, y_kron, (((1, 4), (0, 1)), ((), ())), precision=split_precision
        )
        section = lax.all_to_all(partial_y, "gx", split_axis=0, concat_axis=0, tiled=True)
        summed_x = jnp.einsum("pqkbx,bjxqn->pkjn", x_blocks, section, precision=split_precision)
        summed_x = summed_x.reshape(2, y_parts, kx_local, mode_local, channels * KY)
        summed_x = summed_x.transpose(1, 0, 2, 3, 4)
        gathered = lax.all_to_all(summed_x, "gy", split_axis=0, concat_axis=0, tiled=True)
        summed_y = jnp.sum(gathered, axis=0).reshape(2, kx_local, mode_local, channels, KY)
        return summed_y.transpose(0, 2, 3, 1, 4)

    def full_modes(field):
        planes = field.transpose(1, 0, 2, 3).reshape(x_local, channels * y_local, depth_time)
        spectra = depth_forward(planes).reshape(
            x_groups, 2, mode_local, x_local, channels * y_local
        )
        section = lax.all_to_all(spectra, "gx", split_axis=0, concat_axis=0, tiled=True)
        summed_x = jnp.einsum("pqkbx,bqjxn->pkjn", x_blocks, section, precision=split_precision)
        summed_x = summed_x.reshape(2, y_parts, kx_local, mode_local, channels * y_local)
        summed_x = summed_x.transpose(1, 0, 2, 3, 4)
        gathered = lax.all_to_all(summed_x, "gy", split_axis=0, concat_axis=0, tiled=True)
        gathered = gathered.reshape(gathered.shape[:4] + (channels, y_local))
        return jnp.einsum("pqksy,sqajcy->pjcak", y_split, gathered, precision=split_precision)

    dual_modes = full_modes(cotangent)
    field_spectrum = field_modes(field_in)
    mode_ids = lax.axis_index("gx") * mode_local + lax.iota(jnp.int32, mode_local)
    doubling = jnp.where(mode_ids % MT == 0, 1.0, 2.0).astype(jnp.float32)[:, None, None, None]
    field_real = field_spectrum[0]
    field_imag = field_spectrum[1]
    dual_real = dual_modes[0] * doubling
    dual_imag = dual_modes[1] * doubling
    left = jnp.stack([field_real, field_real])[:, :, :, None]
    left_swap = jnp.stack([field_imag, -field_imag])[:, :, :, None]
    right = jnp.stack([dual_real, dual_imag])[:, :, None]
    right_swap = jnp.stack([dual_imag, dual_real])[:, :, None]
    grad_weight = left * right + left_swap * right_swap
    back_real = spec_weight[0][:, :, 0] * dual_real[:, :1] + spec_weight[1][:, :, 0] * dual_imag[:, :1]
    back_imag = spec_weight[0][:, :, 0] * dual_imag[:, :1] - spec_weight[1][:, :, 0] * dual_real[:, :1]
    for out_channel in range(1, channels):
        weight_real = spec_weight[0][:, :, out_channel]
        weight_imag = spec_weight[1][:, :, out_channel]
        dual_r = dual_real[:, out_channel : out_channel + 1]
        dual_i = dual_imag[:, out_channel : out_channel + 1]
        back_real = back_real + (weight_real * dual_r + weight_imag * dual_i)
        back_imag = back_imag + (weight_real * dual_i - weight_imag * dual_r)
    backward = jnp.stack([back_real, back_imag])
    y_parts = lax.axis_size("gy")
    y_chunks = y_table.reshape(2, 2, KY, y_parts, y_local)
    spread = jnp.einsum("qpkdy,qjcak->dpajcy", y_chunks, backward, precision=split_precision)
    spread = spread.reshape(spread.shape[:4] + (channels * y_local,))
    y_done = lax.all_to_all(spread, "gy", split_axis=0, concat_axis=0, tiled=True)
    x_inverse = x_table.reshape(2, 2, y_parts, KX // y_parts, x_groups, x_local)
    x_spread = jnp.einsum("pqsabx,spajn->bxqjn", x_inverse, y_done, precision=split_precision)
    section = lax.all_to_all(x_spread, "gx", split_axis=0, concat_axis=0, tiled=True)
    depth_parts = depth_flat.reshape(2, x_groups, mode_local, depth_time)
    summed = jnp.einsum("sxqjn,qsjz->xnz", section, depth_parts, precision=split_precision)
    summed = lax.optimization_barrier(summed.astype(jnp.bfloat16))
    grad_field = summed.reshape(x_local, channels, y_local, depth_time).transpose(1, 0, 2, 3)
    return (grad_field, grad_weight)


def solution(mesh):
    in_specs = (
        P(None, "gx", "gy", None),
        P(None, "gx", "gy", None),
        P(None, "gx", None, None, "gy", None),
    )
    out_specs = (P(None, "gx", "gy", None), P(None, "gx", None, None, "gy", None))
    return jax.shard_map(
        layer_body, mesh=mesh, in_specs=in_specs, out_specs=out_specs, check_vma=False
    )
```
